32 devices in a mesh: dp: 8 (over y, x, core), tensor: 4 (over z).
Axes of the slice: x: 2, y: 2, z: 4, core: 2. Of those that a mesh axis runs over, the one named last changes fastest.
Arguments:
- acts: bfloat16 [4096, 2048], P('dp', 'tensor'), may hold values from -6 to 6
- out_grads: bfloat16 [4096, 8192], P('dp', 'tensor'), may hold values from -6 to 6
- basis_out: bfloat16 [8192, 8192], P('tensor'), may hold values from -0.0625 to 0.0625
- basis_in: bfloat16 [2048, 2048], P('tensor'), may hold values from -0.125 to 0.125
- slot_sequence: int32 [16], replicated, may hold values from 0 to 15, each once
- seq_lengths: int32 [16], replicated, may hold values from 1 to 256, 2560 in all
Outputs:
- eigenvalues: float32 [8192, 2048], P('tensor', 'dp')
The draws below stay inside these ranges and needn't reach their ends.
Inputs may be any that keep to these rules, and one draw needn't show every extreme that they name: `slot_sequence`: every sequence number appears exactly once. `seq_lengths`: the largest count is exactly 256.
All inputs are finite; a program needn't handle non-finite values.
Results may differ from the reference program's by a relative error of at most 0.0018.
Values may be sent and summed in bfloat16 or wider, within the bound.
No kernel may reach another device: no remote copies, remote signals or barrier semaphores. Data moves between devices by JAX's collectives and lax.ppermute only.
A program may use at most 128 MiB of HBM per device.

```python
import math
import jax
import jax.numpy as jnp
import numpy as np
from jax import lax

DIN = 2048
DOUT = 8192
LEN = 256
NSEQ = 16
TOKENS = 4096


def shard_levels(key, extent, cuts, low, largest):
    factor_of, own = 1.0, jax.random.fold_in(key, 6)
    for position, parts in cuts:
        heights = jnp.exp(jax.random.uniform(jax.random.fold_in(own, position), (parts,), jnp.float32, low / len(cuts), largest / len(cuts)))
        factor_of = factor_of * jnp.repeat(heights, extent[position] // parts).reshape([-1 if axis == position else 1 for axis in range(len(extent))])
    return factor_of


def length_profile(count, total, reach, lean):
    weights = [(1 << 20) // math.isqrt(standing ** lean) + 1 for standing in range(2, count + 1)]
    rest, counts = total - reach - (count - 1), [1] * (count - 1)
    while rest > 0:
        candidates = [i for i in range(count - 1) if counts[i] < reach]
        whole, remaining = sum([weights[i] for i in candidates]), rest
        for i in candidates:
            extra = min(reach - counts[i], max(1, remaining * weights[i] // whole), rest)
            counts[i] = counts[i] + extra
            rest = rest - extra
    return np.array([reach] + counts)


def ragged_sizes(rng, count, total, most, lean):
    if count == 2:
        one = jax.random.randint(rng, (), max(1, total - most), min(most, total - 1) + 1)
        return jnp.stack([one, total - one])
    sizes = jnp.asarray(length_profile(count, total, most, lean), jnp.int32)
    pairs = (count - 1) // 2
    source_of, taker = sizes[1:1 + 2 * pairs:2], sizes[2:2 + 2 * pairs:2]
    room = jnp.minimum(source_of - 1, most - taker)
    moved = jax.random.randint(jax.random.fold_in(rng, 1), (pairs,), 0, 1 << 20) % (room + 1)
    sizes = sizes.at[1:1 + 2 * pairs:2].set(source_of - moved).at[2:2 + 2 * pairs:2].set(taker + moved)
    return sizes[jax.random.permutation(jax.random.fold_in(rng, 2), count)]


def noise(stream_key, dims, width, reach, shards=(), kind=jnp.bfloat16):
    entries = width * jax.random.normal(stream_key, dims, jnp.float32)
    if shards:
        entries = entries * shard_levels(stream_key, dims, shards, -0.22, 0.18)
    return jnp.clip(entries, -reach, reach).astype(kind)


def setup_inputs(seed: int = 0) -> dict:
    keys = jax.random.split(jax.random.key(seed), 7)
    acts = noise(keys[0], (TOKENS, DIN), 1.0, 6.0, ((0, 8), (1, 4)))
    out_grads = noise(keys[1], (TOKENS, DOUT), 1.0, 6.0, ((0, 8), (1, 4)))
    basis_out = noise(keys[2], (DOUT, DOUT), DOUT ** -0.5, 0.0625, ((0, 4),))
    basis_in = noise(keys[3], (DIN, DIN), DIN ** -0.5, 0.125, ((0, 4),))
    slot_sequence = jax.random.permutation(keys[4], NSEQ).astype(jnp.int32)
    seq_lengths = ragged_sizes(keys[5], NSEQ, NSEQ * LEN * 5 // 8, LEN, 2).astype(jnp.int32)
    return dict(acts=acts, out_grads=out_grads, basis_out=basis_out, basis_in=basis_in, slot_sequence=slot_sequence, seq_lengths=seq_lengths)


def reference(acts, out_grads, basis_out, basis_in, slot_sequence, seq_lengths):
    seq_total = seq_lengths.shape[0]
    slot_counts = seq_lengths[slot_sequence]
    positions = jnp.arange(LEN, dtype=jnp.int32)

    def per_slot(running, slot_id):
        first_row = (slot_id * LEN).astype(jnp.int32)
        act_block = lax.dynamic_slice_in_dim(acts, first_row, LEN, 0)
        grad_block = lax.dynamic_slice_in_dim(out_grads, first_row, LEN, 0)
        valid_mask = positions < slot_counts[slot_id]
        masked = jnp.where(valid_mask[:, None], grad_block, jnp.zeros_like(grad_block))
        rot_grads = jnp.dot(masked, basis_out, preferred_element_type=jnp.float32).astype(jnp.bfloat16)
        rot_acts = jnp.dot(act_block, basis_in, preferred_element_type=jnp.float32).astype(jnp.bfloat16)
        rotated = jnp.dot(rot_grads.T, rot_acts, preferred_element_type=jnp.float32)
        return running + rotated * rotated, None

    start_sum = jnp.zeros((DOUT, DIN), jnp.float32)
    summed, _ = lax.scan(per_slot, start_sum, jnp.arange(seq_total, dtype=jnp.int32))
    return summed / (seq_total * LEN)
```

```python
import jax
import jax.numpy as jnp
from jax import lax
from jax.sharding import PartitionSpec as P

LEN = 256
VALID_NUM, VALID_DEN = 5, 8


def redistribute(x, dp):
    slots = x.shape[0] // LEN
    width = x.shape[1]
    x = x.reshape(slots, LEN // dp, dp, width).transpose(2, 0, 1, 3).reshape(-1, width)
    return lax.all_to_all(x, "dp", 0, 0, tiled=True)


def shards(acts, out_grads, basis_out, basis_in, slot_sequence, seq_lengths, *, dp):
    tok_rows = acts.shape[0]
    local_slots = tok_rows // LEN
    nseq = seq_lengths.shape[0]
    per = LEN // dp
    total = nseq * LEN * VALID_NUM // VALID_DEN
    cap = -(-(total + nseq * (dp - 1)) // dp)
    cap = -(-cap // 16) * 16
    group = lax.axis_index("dp")

    counts = seq_lengths[slot_sequence]
    groups = jnp.arange(dp, dtype=jnp.int32)
    kept = jnp.clip((counts[:, None] - groups[None, :] + dp - 1) // dp, 0, per)
    ends = jnp.cumsum(kept, axis=0)
    starts = ends - kept

    my_ends = ends[:, group]
    my_starts = starts[:, group]
    rows = jnp.arange(cap, dtype=jnp.int32)
    slot_of = jnp.sum((my_ends[None, :] <= rows[:, None]).astype(jnp.int32), axis=1)
    in_use = slot_of < nseq
    slot_c = jnp.minimum(slot_of, nseq - 1)
    src = jnp.clip(slot_c * per + rows - my_starts[slot_c], 0, nseq * per - 1)

    grads_r = redistribute(out_grads, dp)
    grads_p = jnp.take(grads_r, src, axis=0, mode="clip")
    grads_p = jnp.where(in_use[:, None], grads_p, jnp.zeros_like(grads_p))
    acts_r = redistribute(acts, dp)
    acts_p = jnp.take(acts_r, src, axis=0, mode="clip")

    act_part = jnp.dot(acts_p, basis_in, preferred_element_type=jnp.float32)
    in_cols = act_part.shape[1] // dp
    act_part = act_part.reshape(cap, dp, in_cols).transpose(1, 0, 2).reshape(-1, in_cols)
    act_part = lax.all_to_all(act_part, "dp", 0, 0, tiled=True)
    rot_acts = lax.psum(act_part, "tensor").astype(jnp.bfloat16)

    grad_part = jnp.dot(grads_p, basis_out, preferred_element_type=jnp.float32)
    rot_grads = lax.psum_scatter(grad_part, "tensor", scatter_dimension=1, tiled=True)
    rot_grads = rot_grads.astype(jnp.bfloat16)
    all_grads = lax.all_gather(rot_grads, "dp", axis=0, tiled=True)

    js = jnp.arange(per, dtype=jnp.int32)
    pick = groups[None, :, None] * cap + starts[:, :, None] + js[None, None, :]
    live = js[None, None, :] < kept[:, :, None]
    pick = jnp.where(live, pick, 0).reshape(-1)
    live = live.reshape(-1)
    grads_u = jnp.take(all_grads, pick, axis=0, mode="clip")
    acts_u = jnp.take(rot_acts, pick, axis=0, mode="clip")
    acts_u = jnp.where(live[:, None], acts_u, jnp.zeros_like(acts_u))

    squares = jnp.zeros((all_grads.shape[1], rot_acts.shape[1]), jnp.float32)
    for slot in range(nseq):
        g = grads_u[slot * LEN : (slot + 1) * LEN]
        a = acts_u[slot * LEN : (slot + 1) * LEN]
        rotated = lax.dot_general(g, a, (((0,), (0,)), ((), ())), preferred_element_type=jnp.float32)
        squares = squares + rotated * rotated
    return squares / (nseq * LEN)


def solution(mesh):
    dp = mesh.shape["dp"]

    def body(*args):
        return shards(*args, dp=dp)

    return jax.shard_map(
        body,
        mesh=mesh,
        in_specs=(
            P("dp", "tensor"),
            P("dp", "tensor"),
            P("tensor", None),
            P("tensor", None),
            P(),
            P(),
        ),
        out_specs=P("tensor", "dp"),
        check_vma=False,
    )
```

```python
import jax
import jax.numpy as jnp
from jax import lax
from jax.sharding import PartitionSpec as P

LEN = 256
VALID_NUM, VALID_DEN = 5, 8
CHUNKS = 4


def redistribute(x, dp):
    slots = x.shape[0] // LEN
    width = x.shape[1]
    x = x.reshape(slots, LEN // dp, dp, width).transpose(2, 0, 1, 3).reshape(-1, width)
    return lax.all_to_all(x, "dp", 0, 0, tiled=True)


def shards(acts, out_grads, basis_out, basis_in, slot_sequence, seq_lengths, *, dp, tp):
    tok_rows = acts.shape[0]
    nseq = seq_lengths.shape[0]
    per = LEN // dp
    total = nseq * LEN * VALID_NUM // VALID_DEN
    cap = -(-(total + nseq * (dp - 1)) // dp)
    cap = -(-cap // 16) * 16
    rows_all = dp * cap
    group = lax.axis_index("dp")

    counts = seq_lengths[slot_sequence]
    groups = jnp.arange(dp, dtype=jnp.int32)
    kept = jnp.clip((counts[:, None] - groups[None, :] + dp - 1) // dp, 0, per)
    ends = jnp.cumsum(kept, axis=0)
    starts = ends - kept

    my_ends = ends[:, group]
    my_starts = starts[:, group]
    rows = jnp.arange(cap, dtype=jnp.int32)
    slot_of = jnp.sum((my_ends[None, :] <= rows[:, None]).astype(jnp.int32), axis=1)
    in_use = slot_of < nseq
    slot_c = jnp.minimum(slot_of, nseq - 1)
    src = jnp.clip(slot_c * per + rows - my_starts[slot_c], 0, nseq * per - 1)

    grads_r = redistribute(out_grads, dp)
    grads_p = jnp.take(grads_r, src, axis=0, mode="clip")
    grads_p = jnp.where(in_use[:, None], grads_p, jnp.zeros_like(grads_p))
    acts_r = redistribute(acts, dp)
    acts_p = jnp.take(acts_r, src, axis=0, mode="clip")

    act_part = jnp.dot(acts_p, basis_in, preferred_element_type=jnp.float32)
    act_sum = lax.psum_scatter(act_part, "tensor", scatter_dimension=1, tiled=True)
    act_whole = lax.all_gather(act_sum.astype(jnp.bfloat16), "tensor", axis=1, tiled=True)
    in_cols = act_whole.shape[1] // dp
    act_whole = act_whole.reshape(cap, dp, in_cols).transpose(1, 0, 2).reshape(-1, in_cols)
    rot_acts = lax.all_to_all(act_whole, "dp", 0, 0, tiled=True)

    lo = groups[None, :] * cap + starts
    win = jnp.minimum(lo, rows_all - per)
    js = jnp.arange(per, dtype=jnp.int32)
    at = win[:, :, None] + js[None, None, :]
    live = (at >= lo[:, :, None]) & (at < (lo + kept)[:, :, None])

    def windows(rows_of, slot):
        return jnp.concatenate([lax.dynamic_slice_in_dim(rows_of, win[slot, g], per, 0) for g in range(dp)])

    units = cap // 16
    bounds = [16 * (c * units // CHUNKS) for c in range(CHUNKS + 1)]
    pieces = []
    for c in range(CHUNKS):
        if c == 1:
            grads_p, rot_acts = lax.optimization_barrier((grads_p, rot_acts))
        block = grads_p[bounds[c] : bounds[c + 1]]
        grad_part = jnp.dot(block, basis_out, preferred_element_type=jnp.float32)
        rot_grads = lax.psum_scatter(grad_part, "tensor", scatter_dimension=1, tiled=True)
        rot_grads = rot_grads.astype(jnp.bfloat16)
        sent = jnp.broadcast_to(rot_grads[None], (dp,) + rot_grads.shape).reshape(-1, rot_grads.shape[1])
        got = lax.all_to_all(sent, "dp", 0, 0, tiled=True)
        pieces.append(got.reshape(dp, -1, got.shape[1]))
    all_grads = jnp.concatenate(pieces, axis=1).reshape(rows_all, -1)

    def one_slot(slot, squares):
        g_s = windows(all_grads, slot)
        a_s = windows(rot_acts, slot)
        a_s = jnp.where(live[slot].reshape(-1, 1), a_s, jnp.zeros_like(a_s))
        rotated = lax.dot_general(g_s, a_s, (((0,), (0,)), ((), ())), preferred_element_type=jnp.float32)
        return squares + rotated * rotated

    squares = jnp.zeros((all_grads.shape[1], rot_acts.shape[1]), jnp.float32)
    squares = lax.fori_loop(0, nseq, one_slot, squares)
    return squares / (nseq * LEN)


def solution(mesh):
    dp = mesh.shape["dp"]
    tp = mesh.shape["tensor"]

    def body(*args):
        return shards(*args, dp=dp, tp=tp)

    return jax.shard_map(
        body,
        mesh=mesh,
        in_specs=(
            P("dp", "tensor"),
            P("dp", "tensor"),
            P("tensor", None),
            P("tensor", None),
            P(),
            P(),
        ),
        out_specs=P("tensor", "dp"),
        check_vma=False,
    )
```

```python
import jax
import jax.numpy as jnp
from jax import lax
from jax.sharding import PartitionSpec as P

LEN = 256
VALID_NUM, VALID_DEN = 5, 8


def redistribute(x, dp):
    slots = x.shape[0] // LEN
    width = x.shape[1]
    x = x.reshape(slots, LEN // dp, dp, width).transpose(2, 0, 1, 3).reshape(-1, width)
    return lax.all_to_all(x, "dp", 0, 0, tiled=True)


def shards(acts, out_grads, basis_out, basis_in, slot_sequence, seq_lengths, *, dp):
    tok_rows = acts.shape[0]
    local_slots = tok_rows // LEN
    nseq = seq_lengths.shape[0]
    per = LEN // dp
    total = nseq * LEN * VALID_NUM // VALID_DEN
    cap = -(-(total + nseq * (dp - 1)) // dp)
    cap = -(-cap // 16) * 16
    group = lax.axis_index("dp")

    counts = seq_lengths[slot_sequence]
    groups = jnp.arange(dp, dtype=jnp.int32)
    kept = jnp.clip((counts[:, None] - groups[None, :] + dp - 1) // dp, 0, per)
    ends = jnp.cumsum(kept, axis=0)
    starts = ends - kept

    my_ends = ends[:, group]
    my_starts = starts[:, group]
    rows = jnp.arange(cap, dtype=jnp.int32)
    slot_of = jnp.sum((my_ends[None, :] <= rows[:, None]).astype(jnp.int32), axis=1)
    in_use = slot_of < nseq
    slot_c = jnp.minimum(slot_of, nseq - 1)
    src = jnp.clip(slot_c * per + rows - my_starts[slot_c], 0, nseq * per - 1)

    grads_r = redistribute(out_grads, dp)
    grads_p = jnp.take(grads_r, src, axis=0, mode="clip")
    grads_p = jnp.where(in_use[:, None], grads_p, jnp.zeros_like(grads_p))
    acts_r = redistribute(acts, dp)
    acts_p = jnp.take(acts_r, src, axis=0, mode="clip")

    act_part = jnp.dot(acts_p, basis_in, preferred_element_type=jnp.float32)
    act_sum = lax.psum_scatter(act_part, "tensor", scatter_dimension=1, tiled=True)
    act_whole = lax.all_gather(act_sum.astype(jnp.bfloat16), "tensor", axis=1, tiled=True)
    in_cols = act_whole.shape[1] // dp
    act_whole = act_whole.reshape(cap, dp, in_cols).transpose(1, 0, 2).reshape(-1, in_cols)
    rot_acts = lax.all_to_all(act_whole, "dp", 0, 0, tiled=True)

    grad_part = jnp.dot(grads_p, basis_out, preferred_element_type=jnp.float32)
    rot_grads = lax.psum_scatter(grad_part, "tensor", scatter_dimension=1, tiled=True)
    rot_grads = rot_grads.astype(jnp.bfloat16)
    all_grads = lax.all_gather(rot_grads, "dp", axis=0, tiled=True)

    js = jnp.arange(per, dtype=jnp.int32)
    pick = groups[None, :, None] * cap + starts[:, :, None] + js[None, None, :]
    live = js[None, None, :] < kept[:, :, None]
    pick = jnp.where(live, pick, 0).reshape(-1)
    live = live.reshape(-1)
    grads_u = jnp.take(all_grads, pick, axis=0, mode="clip")
    acts_u = jnp.take(rot_acts, pick, axis=0, mode="clip")
    acts_u = jnp.where(live[:, None], acts_u, jnp.zeros_like(acts_u))

    squares = jnp.zeros((all_grads.shape[1], rot_acts.shape[1]), jnp.float32)
    for slot in range(nseq):
        g = grads_u[slot * LEN : (slot + 1) * LEN]
        a = acts_u[slot * LEN : (slot + 1) * LEN]
        rotated = lax.dot_general(g, a, (((0,), (0,)), ((), ())), preferred_element_type=jnp.float32)
        squares = squares + rotated * rotated
    return squares / (nseq * LEN)


def solution(mesh):
    dp = mesh.shape["dp"]

    def body(*args):
        return shards(*args, dp=dp)

    return jax.shard_map(
        body,
        mesh=mesh,
        in_specs=(
            P("dp", "tensor"),
            P("dp", "tensor"),
            P("tensor", None),
            P("tensor", None),
            P(),
            P(),
        ),
        out_specs=P("tensor", "dp"),
        check_vma=False,
    )
```

```python
import functools

import jax
import jax.numpy as jnp
from jax import lax
from jax.experimental import pallas as pl
from jax.experimental.pallas import tpu as pltpu
from jax.sharding import PartitionSpec as P

LEN = 256
VALID_NUM, VALID_DEN = 5, 8


def redistribute(x, dp):
    slots = x.shape[0] // LEN
    width = x.shape[1]
    x = x.reshape(slots, LEN // dp, dp, width).transpose(2, 0, 1, 3).reshape(-1, width)
    return lax.all_to_all(x, "dp", 0, 0, tiled=True)


def slot_squares(win_ref, lo_ref, hi_ref, grads_hbm, acts_hbm, out_ref, gbuf, abuf, sems, *, dp, per, scale):
    s = pl.program_id(0)
    copies = []
    for g in range(dp):
        w = pl.multiple_of(win_ref[s * dp + g], 16)
        cg = pltpu.make_async_copy(grads_hbm.at[pl.ds(w, per)], gbuf.at[pl.ds(g * per, per)], sems.at[0, g])
        ca = pltpu.make_async_copy(acts_hbm.at[pl.ds(w, per)], abuf.at[pl.ds(g * per, per)], sems.at[1, g])
        cg.start()
        ca.start()
        copies += [cg, ca]
    for c in copies:
        c.wait()

    @pl.when(s == 0)
    def _():
        out_ref[...] = jnp.zeros_like(out_ref)

    for g in range(dp):
        w = win_ref[s * dp + g]
        row = w + lax.broadcasted_iota(jnp.int32, (per, 1), 0)
        keep = (row >= lo_ref[s * dp + g]) & (row < hi_ref[s * dp + g])
        a = abuf[pl.ds(g * per, per), :].astype(jnp.float32)
        abuf[pl.ds(g * per, per), :] = jnp.where(keep, a, 0.0).astype(jnp.bfloat16)
    rotated = lax.dot_general(
        gbuf[...], abuf[...], (((0,), (0,)), ((), ())), preferred_element_type=jnp.float32
    )
    out_ref[...] += rotated * rotated

    @pl.when(s == pl.num_programs(0) - 1)
    def _():
        out_ref[...] = out_ref[...] * scale


def shards(acts, out_grads, basis_out, basis_in, slot_sequence, seq_lengths, *, dp):
    tok_rows = acts.shape[0]
    local_slots = tok_rows // LEN
    nseq = seq_lengths.shape[0]
    per = LEN // dp
    total = nseq * LEN * VALID_NUM // VALID_DEN
    cap = -(-(total + nseq * (dp - 1)) // dp)
    cap = -(-cap // 16) * 16
    group = lax.axis_index("dp")

    counts = seq_lengths[slot_sequence]
    groups = jnp.arange(dp, dtype=jnp.int32)
    kept = jnp.clip((counts[:, None] - groups[None, :] + dp - 1) // dp, 0, per)
    ends = jnp.cumsum(kept, axis=0)
    starts = ends - kept

    my_ends = ends[:, group]
    my_starts = starts[:, group]
    rows = jnp.arange(cap, dtype=jnp.int32)
    slot_of = jnp.sum((my_ends[None, :] <= rows[:, None]).astype(jnp.int32), axis=1)
    in_use = slot_of < nseq
    slot_c = jnp.minimum(slot_of, nseq - 1)
    src = jnp.clip(slot_c * per + rows - my_starts[slot_c], 0, nseq * per - 1)

    grads_r = redistribute(out_grads, dp)
    grads_p = jnp.take(grads_r, src, axis=0, mode="clip")
    grads_p = jnp.where(in_use[:, None], grads_p, jnp.zeros_like(grads_p))
    acts_r = redistribute(acts, dp)
    acts_p = jnp.take(acts_r, src, axis=0, mode="clip")

    act_part = jnp.dot(acts_p, basis_in, preferred_element_type=jnp.float32)
    act_sum = lax.psum_scatter(act_part, "tensor", scatter_dimension=1, tiled=True)
    act_whole = lax.all_gather(act_sum.astype(jnp.bfloat16), "tensor", axis=1, tiled=True)
    grads_p, act_whole = lax.optimization_barrier((grads_p, act_whole))
    in_cols = act_whole.shape[1] // dp
    act_whole = act_whole.reshape(cap, dp, in_cols).transpose(1, 0, 2).reshape(-1, in_cols)
    rot_acts = lax.all_to_all(act_whole, "dp", 0, 0, tiled=True)

    grad_part = jnp.dot(grads_p, basis_out, preferred_element_type=jnp.float32)
    rot_grads = lax.psum_scatter(grad_part, "tensor", scatter_dimension=1, tiled=True)
    rot_grads = rot_grads.astype(jnp.bfloat16)
    all_grads = lax.all_gather(rot_grads, "dp", axis=0, tiled=True)

    span = per + 16
    lo = groups[None, :] * cap + starts
    win = jnp.minimum((lo // 16) * 16, dp * cap - span)
    out_rows, in_cols = all_grads.shape[1], rot_acts.shape[1]
    kernel = functools.partial(slot_squares, dp=dp, per=span, scale=1.0 / (nseq * LEN))
    return pl.pallas_call(
        kernel,
        out_shape=jax.ShapeDtypeStruct((out_rows, in_cols), jnp.float32),
        grid_spec=pltpu.PrefetchScalarGridSpec(
            num_scalar_prefetch=3,
            grid=(nseq,),
            in_specs=[pl.BlockSpec(memory_space=pl.ANY), pl.BlockSpec(memory_space=pl.ANY)],
            out_specs=pl.BlockSpec((out_rows, in_cols), lambda s, *_: (0, 0)),
            scratch_shapes=[
                pltpu.VMEM((dp * span, out_rows), jnp.bfloat16),
                pltpu.VMEM((dp * span, in_cols), jnp.bfloat16),
                pltpu.SemaphoreType.DMA((2, dp)),
            ],
        ),
        compiler_params=pltpu.CompilerParams(dimension_semantics=("arbitrary",)),
    )(win.reshape(-1), lo.reshape(-1), (lo + kept).reshape(-1), all_grads, rot_acts)


def solution(mesh):
    dp = mesh.shape["dp"]

    def body(*args):
        return shards(*args, dp=dp)

    return jax.shard_map(
        body,
        mesh=mesh,
        in_specs=(
            P("dp", "tensor"),
            P("dp", "tensor"),
            P("tensor", None),
            P("tensor", None),
            P(),
            P(),
        ),
        out_specs=P("tensor", "dp"),
        check_vma=False,
    )
```

```python
import functools

import jax
import jax.numpy as jnp
from jax import lax
from jax.experimental import pallas as pl
from jax.experimental.pallas import tpu as pltpu
from jax.sharding import PartitionSpec as P

LEN = 256
VALID_NUM, VALID_DEN = 5, 8


def redistribute(x, dp):
    slots = x.shape[0] // LEN
    width = x.shape[1]
    x = x.reshape(slots, LEN // dp, dp, width).transpose(2, 0, 1, 3).reshape(-1, width)
    return lax.all_to_all(x, "dp", 0, 0, tiled=True)


def slot_squares(win_ref, lo_ref, hi_ref, grads_hbm, acts_hbm, out_ref, gbuf, abuf, sems, *, dp, per, pair, scale):
    s = pl.program_id(0)
    n = pl.num_programs(0)

    def copies(step, b):
        out = []
        for q in range(pair):
            for g in range(dp):
                w = pl.multiple_of(win_ref[(step * pair + q) * dp + g], 16)
                rows = pl.ds(g * per, per)
                out.append(pltpu.make_async_copy(grads_hbm.at[pl.ds(w, per)], gbuf.at[b, q, rows], sems.at[b, q, 0, g]))
                out.append(pltpu.make_async_copy(acts_hbm.at[pl.ds(w, per)], abuf.at[b, q, rows], sems.at[b, q, 1, g]))
        return out

    b = s % 2

    @pl.when(s == 0)
    def _():
        for c in copies(0, 0):
            c.start()

    @pl.when(s + 1 < n)
    def _():
        for c in copies(s + 1, 1 - b):
            c.start()

    for c in copies(s, b):
        c.wait()

    @pl.when(s == 0)
    def _():
        out_ref[...] = jnp.zeros_like(out_ref)

    acc = None
    for q in range(pair):
        slot = s * pair + q
        for g in range(dp):
            row = win_ref[slot * dp + g] + lax.broadcasted_iota(jnp.int32, (per, 1), 0)
            keep = (row >= lo_ref[slot * dp + g]) & (row < hi_ref[slot * dp + g])
            a = abuf[b, q, pl.ds(g * per, per), :].astype(jnp.float32)
            abuf[b, q, pl.ds(g * per, per), :] = jnp.where(keep, a, 0.0).astype(jnp.bfloat16)
        rotated = lax.dot_general(
            gbuf[b, q], abuf[b, q], (((0,), (0,)), ((), ())), preferred_element_type=jnp.float32
        )
        acc = rotated * rotated if acc is None else acc + rotated * rotated
    out_ref[...] += acc

    @pl.when(s == n - 1)
    def _():
        out_ref[...] = out_ref[...] * scale


def shards(acts, out_grads, basis_out, basis_in, slot_sequence, seq_lengths, *, dp):
    tok_rows = acts.shape[0]
    local_slots = tok_rows // LEN
    nseq = seq_lengths.shape[0]
    per = LEN // dp
    total = nseq * LEN * VALID_NUM // VALID_DEN
    cap = -(-(total + nseq * (dp - 1)) // dp)
    cap = -(-cap // 16) * 16
    group = lax.axis_index("dp")

    counts = seq_lengths[slot_sequence]
    groups = jnp.arange(dp, dtype=jnp.int32)
    kept = jnp.clip((counts[:, None] - groups[None, :] + dp - 1) // dp, 0, per)
    ends = jnp.cumsum(kept, axis=0)
    starts = ends - kept

    my_ends = ends[:, group]
    my_starts = starts[:, group]
    rows = jnp.arange(cap, dtype=jnp.int32)
    slot_of = jnp.sum((my_ends[None, :] <= rows[:, None]).astype(jnp.int32), axis=1)
    in_use = slot_of < nseq
    slot_c = jnp.minimum(slot_of, nseq - 1)
    src = jnp.clip(slot_c * per + rows - my_starts[slot_c], 0, nseq * per - 1)

    grads_r = redistribute(out_grads, dp)
    grads_p = jnp.take(grads_r, src, axis=0, mode="clip")
    grads_p = jnp.where(in_use[:, None], grads_p, jnp.zeros_like(grads_p))
    acts_r = redistribute(acts, dp)
    acts_p = jnp.take(acts_r, src, axis=0, mode="clip")

    act_part = jnp.dot(acts_p, basis_in, preferred_element_type=jnp.float32)
    act_sum = lax.psum_scatter(act_part, "tensor", scatter_dimension=1, tiled=True)
    act_whole = lax.all_gather(act_sum.astype(jnp.bfloat16), "tensor", axis=1, tiled=True)
    grad_part = jnp.dot(grads_p, basis_out, preferred_element_type=jnp.float32)
    grad_part, act_whole = lax.optimization_barrier((grad_part, act_whole))
    in_cols = act_whole.shape[1] // dp
    act_whole = act_whole.reshape(cap, dp, in_cols).transpose(1, 0, 2).reshape(-1, in_cols)
    rot_acts = lax.all_to_all(act_whole, "dp", 0, 0, tiled=True)

    rot_grads = lax.psum_scatter(grad_part, "tensor", scatter_dimension=1, tiled=True)
    rot_grads = rot_grads.astype(jnp.bfloat16)
    all_grads = lax.all_gather(rot_grads, "dp", axis=0, tiled=True)

    span = per + 16
    lo = groups[None, :] * cap + starts
    win = jnp.minimum((lo // 16) * 16, dp * cap - span)
    out_rows, in_cols = all_grads.shape[1], rot_acts.shape[1]
    pair = 2 if nseq % 2 == 0 else 1
    kernel = functools.partial(slot_squares, dp=dp, per=span, pair=pair, scale=1.0 / (nseq * LEN))
    return pl.pallas_call(
        kernel,
        out_shape=jax.ShapeDtypeStruct((out_rows, in_cols), jnp.float32),
        grid_spec=pltpu.PrefetchScalarGridSpec(
            num_scalar_prefetch=3,
            grid=(nseq // pair,),
            in_specs=[pl.BlockSpec(memory_space=pl.ANY), pl.BlockSpec(memory_space=pl.ANY)],
            out_specs=pl.BlockSpec((out_rows, in_cols), lambda s, *_: (0, 0)),
            scratch_shapes=[
                pltpu.VMEM((2, pair, dp * span, out_rows), jnp.bfloat16),
                pltpu.VMEM((2, pair, dp * span, in_cols), jnp.bfloat16),
                pltpu.SemaphoreType.DMA((2, pair, 2, dp)),
            ],
        ),
        compiler_params=pltpu.CompilerParams(dimension_semantics=("arbitrary",)),
    )(win.reshape(-1), lo.reshape(-1), (lo + kept).reshape(-1), all_grads, rot_acts)


def solution(mesh):
    dp = mesh.shape["dp"]

    def body(*args):
        return shards(*args, dp=dp)

    return jax.shard_map(
        body,
        mesh=mesh,
        in_specs=(
            P("dp", "tensor"),
            P("dp", "tensor"),
            P("tensor", None),
            P("tensor", None),
            P(),
            P(),
        ),
        out_specs=P("tensor", "dp"),
        check_vma=False,
    )
```

```python
import functools

import jax
import jax.numpy as jnp
from jax import lax
from jax.experimental import pallas as pl
from jax.experimental.pallas import tpu as pltpu
from jax.sharding import PartitionSpec as P

LEN = 256
VALID_NUM, VALID_DEN = 5, 8


def redistribute(x, dp):
    slots = x.shape[0] // LEN
    width = x.shape[1]
    x = x.reshape(slots, LEN // dp, dp, width).transpose(2, 0, 1, 3).reshape(-1, width)
    return lax.all_to_all(x, "dp", 0, 0, tiled=True)


def slot_squares(win_ref, lo_ref, hi_ref, grads_hbm, acts_hbm, out_ref, gbuf, abuf, sems, *, dp, per, pair, scale):
    s = pl.program_id(0)
    n = pl.num_programs(0)

    def copies(step, b):
        out = []
        for q in range(pair):
            for g in range(dp):
                w = pl.multiple_of(win_ref[(step * pair + q) * dp + g], 16)
                rows = pl.ds(g * per, per)
                out.append(pltpu.make_async_copy(grads_hbm.at[pl.ds(w, per)], gbuf.at[b, q, rows], sems.at[b, q, 0, g]))
                out.append(pltpu.make_async_copy(acts_hbm.at[pl.ds(w, per)], abuf.at[b, q, rows], sems.at[b, q, 1, g]))
        return out

    b = s % 2

    @pl.when(s == 0)
    def _():
        for c in copies(0, 0):
            c.start()

    @pl.when(s + 1 < n)
    def _():
        for c in copies(s + 1, 1 - b):
            c.start()

    for c in copies(s, b):
        c.wait()

    @pl.when(s == 0)
    def _():
        out_ref[...] = jnp.zeros_like(out_ref)

    acc = None
    for q in range(pair):
        slot = s * pair + q
        for g in range(dp):
            row = win_ref[slot * dp + g] + lax.broadcasted_iota(jnp.int32, (per, 1), 0)
            keep = (row >= lo_ref[slot * dp + g]) & (row < hi_ref[slot * dp + g])
            a = abuf[b, q, pl.ds(g * per, per), :].astype(jnp.float32)
            abuf[b, q, pl.ds(g * per, per), :] = jnp.where(keep, a, 0.0).astype(jnp.bfloat16)
        rotated = lax.dot_general(
            gbuf[b, q], abuf[b, q], (((0,), (0,)), ((), ())), preferred_element_type=jnp.float32
        )
        acc = rotated * rotated if acc is None else acc + rotated * rotated
    out_ref[...] += acc

    @pl.when(s == n - 1)
    def _():
        out_ref[...] = out_ref[...] * scale


def shards(acts, out_grads, basis_out, basis_in, slot_sequence, seq_lengths, *, dp):
    tok_rows = acts.shape[0]
    local_slots = tok_rows // LEN
    nseq = seq_lengths.shape[0]
    per = LEN // dp
    total = nseq * LEN * VALID_NUM // VALID_DEN
    cap = -(-(total + nseq * (dp - 1)) // dp)
    cap = -(-cap // 16) * 16
    group = lax.axis_index("dp")

    counts = seq_lengths[slot_sequence]
    groups = jnp.arange(dp, dtype=jnp.int32)
    kept = jnp.clip((counts[:, None] - groups[None, :] + dp - 1) // dp, 0, per)
    ends = jnp.cumsum(kept, axis=0)
    starts = ends - kept

    my_ends = ends[:, group]
    my_starts = starts[:, group]
    rows = jnp.arange(cap, dtype=jnp.int32)
    slot_of = jnp.sum((my_ends[None, :] <= rows[:, None]).astype(jnp.int32), axis=1)
    in_use = slot_of < nseq
    slot_c = jnp.minimum(slot_of, nseq - 1)
    src = jnp.clip(slot_c * per + rows - my_starts[slot_c], 0, nseq * per - 1)

    grads_r = redistribute(out_grads, dp)
    grads_p = jnp.take(grads_r, src, axis=0, mode="clip")
    grads_p = jnp.where(in_use[:, None], grads_p, jnp.zeros_like(grads_p))
    acts_r = redistribute(acts, dp)
    acts_p = jnp.take(acts_r, src, axis=0, mode="clip")

    act_part = jnp.dot(acts_p, basis_in, preferred_element_type=jnp.float32)
    act_sum = lax.psum_scatter(act_part, "tensor", scatter_dimension=1, tiled=True)
    act_whole = lax.all_gather(act_sum.astype(jnp.bfloat16), "tensor", axis=1, tiled=True)
    grad_part = jnp.dot(grads_p, basis_out, preferred_element_type=jnp.float32)
    grad_part, act_whole = lax.optimization_barrier((grad_part, act_whole))
    in_cols = act_whole.shape[1] // dp
    act_whole = act_whole.reshape(cap, dp, in_cols).transpose(1, 0, 2).reshape(-1, in_cols)
    rot_acts = lax.all_to_all(act_whole, "dp", 0, 0, tiled=True)

    rot_grads = lax.psum_scatter(grad_part, "tensor", scatter_dimension=1, tiled=True)
    rot_grads, rot_acts = lax.optimization_barrier((rot_grads, rot_acts))
    rot_grads = rot_grads.astype(jnp.bfloat16)
    all_grads = lax.all_gather(rot_grads, "dp", axis=0, tiled=True)

    span = per + 16
    lo = groups[None, :] * cap + starts
    win = jnp.minimum((lo // 16) * 16, dp * cap - span)
    out_rows, in_cols = all_grads.shape[1], rot_acts.shape[1]
    pair = 2 if nseq % 2 == 0 else 1
    kernel = functools.partial(slot_squares, dp=dp, per=span, pair=pair, scale=1.0 / (nseq * LEN))
    return pl.pallas_call(
        kernel,
        out_shape=jax.ShapeDtypeStruct((out_rows, in_cols), jnp.float32),
        grid_spec=pltpu.PrefetchScalarGridSpec(
            num_scalar_prefetch=3,
            grid=(nseq // pair,),
            in_specs=[pl.BlockSpec(memory_space=pl.ANY), pl.BlockSpec(memory_space=pl.ANY)],
            out_specs=pl.BlockSpec((out_rows, in_cols), lambda s, *_: (0, 0)),
            scratch_shapes=[
                pltpu.VMEM((2, pair, dp * span, out_rows), jnp.bfloat16),
                pltpu.VMEM((2, pair, dp * span, in_cols), jnp.bfloat16),
                pltpu.SemaphoreType.DMA((2, pair, 2, dp)),
            ],
        ),
        compiler_params=pltpu.CompilerParams(dimension_semantics=("arbitrary",)),
    )(win.reshape(-1), lo.reshape(-1), (lo + kept).reshape(-1), all_grads, rot_acts)


def solution(mesh):
    dp = mesh.shape["dp"]

    def body(*args):
        return shards(*args, dp=dp)

    return jax.shard_map(
        body,
        mesh=mesh,
        in_specs=(
            P("dp", "tensor"),
            P("dp", "tensor"),
            P("tensor", None),
            P("tensor", None),
            P(),
            P(),
        ),
        out_specs=P("tensor", "dp"),
        check_vma=False,
    )
```

```python
import functools

import jax
import jax.numpy as jnp
from jax import lax
from jax.experimental import pallas as pl
from jax.experimental.pallas import tpu as pltpu
from jax.sharding import PartitionSpec as P

LEN = 256
VALID_NUM, VALID_DEN = 5, 8


def redistribute(x, dp):
    slots = x.shape[0] // LEN
    width = x.shape[1]
    x = x.reshape(slots, LEN // dp, dp, width).transpose(2, 0, 1, 3).reshape(-1, width)
    return lax.all_to_all(x, "dp", 0, 0, tiled=True)


def slot_squares(win_ref, lo_ref, hi_ref, grads_hbm, acts_hbm, out_ref, gbuf, abuf, sems, *, dp, per, pair, scale):
    s = pl.program_id(0)
    n = pl.num_programs(0)

    def copies(step, b):
        out = []
        for q in range(pair):
            for g in range(dp):
                w = pl.multiple_of(win_ref[(step * pair + q) * dp + g], 16)
                rows = pl.ds(g * per, per)
                out.append(pltpu.make_async_copy(grads_hbm.at[pl.ds(w, per)], gbuf.at[b, q, rows], sems.at[b, q, 0, g]))
                out.append(pltpu.make_async_copy(acts_hbm.at[pl.ds(w, per)], abuf.at[b, q, rows], sems.at[b, q, 1, g]))
        return out

    b = s % 2

    @pl.when(s == 0)
    def _():
        for c in copies(0, 0):
            c.start()

    @pl.when(s + 1 < n)
    def _():
        for c in copies(s + 1, 1 - b):
            c.start()

    for c in copies(s, b):
        c.wait()

    @pl.when(s == 0)
    def _():
        out_ref[...] = jnp.zeros_like(out_ref)

    acc = None
    for q in range(pair):
        slot = s * pair + q
        for g in range(dp):
            row = win_ref[slot * dp + g] + lax.broadcasted_iota(jnp.int32, (per, 1), 0)
            keep = (row >= lo_ref[slot * dp + g]) & (row < hi_ref[slot * dp + g])
            a = abuf[b, q, pl.ds(g * per, per), :].astype(jnp.float32)
            abuf[b, q, pl.ds(g * per, per), :] = jnp.where(keep, a, 0.0).astype(jnp.bfloat16)
        rotated = lax.dot_general(
            gbuf[b, q], abuf[b, q], (((0,), (0,)), ((), ())), preferred_element_type=jnp.float32
        )
        acc = rotated * rotated if acc is None else acc + rotated * rotated
    out_ref[...] += acc

    @pl.when(s == n - 1)
    def _():
        out_ref[...] = out_ref[...] * scale


def shards(acts, out_grads, basis_out, basis_in, slot_sequence, seq_lengths, *, dp, tp):
    tok_rows = acts.shape[0]
    local_slots = tok_rows // LEN
    nseq = seq_lengths.shape[0]
    per = LEN // dp
    total = nseq * LEN * VALID_NUM // VALID_DEN
    cap = -(-(total + nseq * (dp - 1)) // dp)
    cap = -(-cap // 16) * 16
    group = lax.axis_index("dp")

    counts = seq_lengths[slot_sequence]
    groups = jnp.arange(dp, dtype=jnp.int32)
    kept = jnp.clip((counts[:, None] - groups[None, :] + dp - 1) // dp, 0, per)
    ends = jnp.cumsum(kept, axis=0)
    starts = ends - kept

    my_ends = ends[:, group]
    my_starts = starts[:, group]
    rows = jnp.arange(cap, dtype=jnp.int32)
    slot_of = jnp.sum((my_ends[None, :] <= rows[:, None]).astype(jnp.int32), axis=1)
    in_use = slot_of < nseq
    slot_c = jnp.minimum(slot_of, nseq - 1)
    src = jnp.clip(slot_c * per + rows - my_starts[slot_c], 0, nseq * per - 1)

    grads_r = redistribute(out_grads, dp)
    grads_p = jnp.take(grads_r, src, axis=0, mode="clip")
    grads_p = jnp.where(in_use[:, None], grads_p, jnp.zeros_like(grads_p))
    acts_r = redistribute(acts, dp)
    acts_p = jnp.take(acts_r, src, axis=0, mode="clip")

    act_part = jnp.dot(acts_p, basis_in, preferred_element_type=jnp.float32)
    quarter = act_part.shape[1] // tp
    blocks = act_part.reshape(cap, tp, quarter).transpose(1, 0, 2).reshape(-1, quarter)
    act_sum = jnp.sum(lax.all_to_all(blocks, "tensor", 0, 0, tiled=True).reshape(tp, cap, quarter), axis=0)
    act_sum = act_sum.astype(jnp.bfloat16)
    sent = jnp.broadcast_to(act_sum[None], (tp,) + act_sum.shape).reshape(-1, quarter)
    act_whole = lax.all_to_all(sent, "tensor", 0, 0, tiled=True).reshape(tp, cap, quarter)
    act_whole = act_whole.transpose(1, 0, 2).reshape(cap, tp * quarter)
    grad_part = jnp.dot(grads_p, basis_out, preferred_element_type=jnp.float32)
    in_cols = act_whole.shape[1] // dp
    act_whole = act_whole.reshape(cap, dp, in_cols).transpose(1, 0, 2).reshape(-1, in_cols)
    rot_acts = lax.all_to_all(act_whole, "dp", 0, 0, tiled=True)

    rot_grads = lax.psum_scatter(grad_part, "tensor", scatter_dimension=1, tiled=True)
    rot_grads, rot_acts = lax.optimization_barrier((rot_grads, rot_acts))
    rot_grads = rot_grads.astype(jnp.bfloat16)
    all_grads = lax.all_gather(rot_grads, "dp", axis=0, tiled=True)

    span = per + 16
    lo = groups[None, :] * cap + starts
    win = jnp.minimum((lo // 16) * 16, dp * cap - span)
    out_rows, in_cols = all_grads.shape[1], rot_acts.shape[1]
    pair = 2 if nseq % 2 == 0 else 1
    kernel = functools.partial(slot_squares, dp=dp, per=span, pair=pair, scale=1.0 / (nseq * LEN))
    return pl.pallas_call(
        kernel,
        out_shape=jax.ShapeDtypeStruct((out_rows, in_cols), jnp.float32),
        grid_spec=pltpu.PrefetchScalarGridSpec(
            num_scalar_prefetch=3,
            grid=(nseq // pair,),
            in_specs=[pl.BlockSpec(memory_space=pl.ANY), pl.BlockSpec(memory_space=pl.ANY)],
            out_specs=pl.BlockSpec((out_rows, in_cols), lambda s, *_: (0, 0)),
            scratch_shapes=[
                pltpu.VMEM((2, pair, dp * span, out_rows), jnp.bfloat16),
                pltpu.VMEM((2, pair, dp * span, in_cols), jnp.bfloat16),
                pltpu.SemaphoreType.DMA((2, pair, 2, dp)),
            ],
        ),
        compiler_params=pltpu.CompilerParams(dimension_semantics=("arbitrary",)),
    )(win.reshape(-1), lo.reshape(-1), (lo + kept).reshape(-1), all_grads, rot_acts)


def solution(mesh):
    dp = mesh.shape["dp"]
    tp = mesh.shape["tensor"]

    def body(*args):
        return shards(*args, dp=dp, tp=tp)

    return jax.shard_map(
        body,
        mesh=mesh,
        in_specs=(
            P("dp", "tensor"),
            P("dp", "tensor"),
            P("tensor", None),
            P("tensor", None),
            P(),
            P(),
        ),
        out_specs=P("tensor", "dp"),
        check_vma=False,
    )
```

```python
import functools

import jax
import jax.numpy as jnp
from jax import lax
from jax.experimental import pallas as pl
from jax.experimental.pallas import tpu as pltpu
from jax.sharding import PartitionSpec as P

LEN = 256
VALID_NUM, VALID_DEN = 5, 8


def redistribute(x, dp):
    slots = x.shape[0] // LEN
    width = x.shape[1]
    x = x.reshape(slots, LEN // dp, dp, width).transpose(2, 0, 1, 3).reshape(-1, width)
    return lax.all_to_all(x, "dp", 0, 0, tiled=True)


def slot_squares(win_ref, lo_ref, hi_ref, grads_hbm, acts_hbm, out_ref, gbuf, abuf, sems, *, dp, per, pair, scale):
    s = pl.program_id(0)
    n = pl.num_programs(0)

    def copies(step, b):
        out = []
        for q in range(pair):
            for g in range(dp):
                w = pl.multiple_of(win_ref[(step * pair + q) * dp + g], 16)
                rows = pl.ds(g * per, per)
                out.append(pltpu.make_async_copy(grads_hbm.at[pl.ds(w, per)], gbuf.at[b, q, rows], sems.at[b, q, 0, g]))
                out.append(pltpu.make_async_copy(acts_hbm.at[pl.ds(w, per)], abuf.at[b, q, rows], sems.at[b, q, 1, g]))
        return out

    b = s % 2

    @pl.when(s == 0)
    def _():
        for c in copies(0, 0):
            c.start()

    @pl.when(s + 1 < n)
    def _():
        for c in copies(s + 1, 1 - b):
            c.start()

    for c in copies(s, b):
        c.wait()

    @pl.when(s == 0)
    def _():
        out_ref[...] = jnp.zeros_like(out_ref)

    acc = None
    for q in range(pair):
        slot = s * pair + q
        for g in range(dp):
            row = win_ref[slot * dp + g] + lax.broadcasted_iota(jnp.int32, (per, 1), 0)
            keep = (row >= lo_ref[slot * dp + g]) & (row < hi_ref[slot * dp + g])
            a = abuf[b, q, pl.ds(g * per, per), :].astype(jnp.float32)
            abuf[b, q, pl.ds(g * per, per), :] = jnp.where(keep, a, 0.0).astype(jnp.bfloat16)
        rotated = lax.dot_general(
            gbuf[b, q], abuf[b, q], (((0,), (0,)), ((), ())), preferred_element_type=jnp.float32
        )
        acc = rotated * rotated if acc is None else acc + rotated * rotated
    out_ref[...] += acc

    @pl.when(s == n - 1)
    def _():
        out_ref[...] = out_ref[...] * scale


def shards(acts, out_grads, basis_out, basis_in, slot_sequence, seq_lengths, *, dp, tp):
    tok_rows = acts.shape[0]
    local_slots = tok_rows // LEN
    nseq = seq_lengths.shape[0]
    per = LEN // dp
    total = nseq * LEN * VALID_NUM // VALID_DEN
    cap = -(-(total + nseq * (dp - 1)) // dp)
    cap = -(-cap // 16) * 16
    group = lax.axis_index("dp")

    counts = seq_lengths[slot_sequence]
    groups = jnp.arange(dp, dtype=jnp.int32)
    kept = jnp.clip((counts[:, None] - groups[None, :] + dp - 1) // dp, 0, per)
    ends = jnp.cumsum(kept, axis=0)
    starts = ends - kept

    my_ends = ends[:, group]
    my_starts = starts[:, group]
    rows = jnp.arange(cap, dtype=jnp.int32)
    slot_of = jnp.sum((my_ends[None, :] <= rows[:, None]).astype(jnp.int32), axis=1)
    in_use = slot_of < nseq
    slot_c = jnp.minimum(slot_of, nseq - 1)
    src = jnp.clip(slot_c * per + rows - my_starts[slot_c], 0, nseq * per - 1)

    grads_r = redistribute(out_grads, dp)
    grads_p = jnp.take(grads_r, src, axis=0, mode="clip")
    grads_p = jnp.where(in_use[:, None], grads_p, jnp.zeros_like(grads_p))
    acts_r = redistribute(acts, dp)
    acts_p = jnp.take(acts_r, src, axis=0, mode="clip")

    quarter = basis_in.shape[1] // tp
    basis_cols = basis_in.reshape(basis_in.shape[0], tp, quarter).transpose(1, 0, 2).reshape(-1, quarter)
    basis_q = lax.all_to_all(basis_cols, "tensor", 0, 0, tiled=True)
    acts_full = lax.all_gather(acts_p, "tensor", axis=1, tiled=True)
    act_q = jnp.dot(acts_full, basis_q, preferred_element_type=jnp.float32).astype(jnp.bfloat16)
    act_whole = lax.all_gather(act_q, "tensor", axis=1, tiled=True)
    grad_part = jnp.dot(grads_p, basis_out, preferred_element_type=jnp.float32)
    grad_part, act_whole = lax.optimization_barrier((grad_part, act_whole))
    in_cols = act_whole.shape[1] // dp
    act_whole = act_whole.reshape(cap, dp, in_cols).transpose(1, 0, 2).reshape(-1, in_cols)
    rot_acts = lax.all_to_all(act_whole, "dp", 0, 0, tiled=True)

    rot_grads = lax.psum_scatter(grad_part, "tensor", scatter_dimension=1, tiled=True)
    rot_grads, rot_acts = lax.optimization_barrier((rot_grads, rot_acts))
    rot_grads = rot_grads.astype(jnp.bfloat16)
    all_grads = lax.all_gather(rot_grads, "dp", axis=0, tiled=True)

    span = per + 16
    lo = groups[None, :] * cap + starts
    win = jnp.minimum((lo // 16) * 16, dp * cap - span)
    out_rows, in_cols = all_grads.shape[1], rot_acts.shape[1]
    pair = 2 if nseq % 2 == 0 else 1
    kernel = functools.partial(slot_squares, dp=dp, per=span, pair=pair, scale=1.0 / (nseq * LEN))
    return pl.pallas_call(
        kernel,
        out_shape=jax.ShapeDtypeStruct((out_rows, in_cols), jnp.float32),
        grid_spec=pltpu.PrefetchScalarGridSpec(
            num_scalar_prefetch=3,
            grid=(nseq // pair,),
            in_specs=[pl.BlockSpec(memory_space=pl.ANY), pl.BlockSpec(memory_space=pl.ANY)],
            out_specs=pl.BlockSpec((out_rows, in_cols), lambda s, *_: (0, 0)),
            scratch_shapes=[
                pltpu.VMEM((2, pair, dp * span, out_rows), jnp.bfloat16),
                pltpu.VMEM((2, pair, dp * span, in_cols), jnp.bfloat16),
                pltpu.SemaphoreType.DMA((2, pair, 2, dp)),
            ],
        ),
        compiler_params=pltpu.CompilerParams(dimension_semantics=("arbitrary",)),
    )(win.reshape(-1), lo.reshape(-1), (lo + kept).reshape(-1), all_grads, rot_acts)


def solution(mesh):
    dp = mesh.shape["dp"]
    tp = mesh.shape["tensor"]

    def body(*args):
        return shards(*args, dp=dp, tp=tp)

    return jax.shard_map(
        body,
        mesh=mesh,
        in_specs=(
            P("dp", "tensor"),
            P("dp", "tensor"),
            P("tensor", None),
            P("tensor", None),
            P(),
            P(),
        ),
        out_specs=P("tensor", "dp"),
        check_vma=False,
    )
```

```python
import functools

import jax
import jax.numpy as jnp
from jax import lax
from jax.experimental import pallas as pl
from jax.experimental.pallas import tpu as pltpu
from jax.sharding import PartitionSpec as P

LEN = 256
VALID_NUM, VALID_DEN = 5, 8


def redistribute(x, dp):
    slots = x.shape[0] // LEN
    width = x.shape[1]
    x = x.reshape(slots, LEN // dp, dp, width).transpose(2, 0, 1, 3).reshape(-1, width)
    return lax.all_to_all(x, "dp", 0, 0, tiled=True)


def slot_squares(win_ref, lo_ref, hi_ref, grads_hbm, acts_hbm, out_ref, gbuf, abuf, sems, *, dp, per, pair, scale):
    s = pl.program_id(0)
    n = pl.num_programs(0)

    def copies(step, b):
        out = []
        for q in range(pair):
            for g in range(dp):
                w = pl.multiple_of(win_ref[(step * pair + q) * dp + g], 16)
                rows = pl.ds(g * per, per)
                out.append(pltpu.make_async_copy(grads_hbm.at[pl.ds(w, per)], gbuf.at[b, q, rows], sems.at[b, q, 0, g]))
                out.append(pltpu.make_async_copy(acts_hbm.at[pl.ds(w, per)], abuf.at[b, q, rows], sems.at[b, q, 1, g]))
        return out

    b = s % 2

    @pl.when(s == 0)
    def _():
        for c in copies(0, 0):
            c.start()

    @pl.when(s + 1 < n)
    def _():
        for c in copies(s + 1, 1 - b):
            c.start()

    for c in copies(s, b):
        c.wait()

    @pl.when(s == 0)
    def _():
        out_ref[...] = jnp.zeros_like(out_ref)

    acc = None
    for q in range(pair):
        slot = s * pair + q
        for g in range(dp):
            row = win_ref[slot * dp + g] + lax.broadcasted_iota(jnp.int32, (per, 1), 0)
            keep = (row >= lo_ref[slot * dp + g]) & (row < hi_ref[slot * dp + g])
            a = abuf[b, q, pl.ds(g * per, per), :].astype(jnp.float32)
            abuf[b, q, pl.ds(g * per, per), :] = jnp.where(keep, a, 0.0).astype(jnp.bfloat16)
        rotated = lax.dot_general(
            gbuf[b, q], abuf[b, q], (((0,), (0,)), ((), ())), preferred_element_type=jnp.float32
        )
        acc = rotated * rotated if acc is None else acc + rotated * rotated
    out_ref[...] += acc

    @pl.when(s == n - 1)
    def _():
        out_ref[...] = out_ref[...] * scale


def shards(acts, out_grads, basis_out, basis_in, slot_sequence, seq_lengths, *, dp, tp):
    tok_rows = acts.shape[0]
    local_slots = tok_rows // LEN
    nseq = seq_lengths.shape[0]
    per = LEN // dp
    total = nseq * LEN * VALID_NUM // VALID_DEN
    cap = -(-(total + nseq * (dp - 1)) // dp)
    cap = -(-cap // 16) * 16
    group = lax.axis_index("dp")

    counts = seq_lengths[slot_sequence]
    groups = jnp.arange(dp, dtype=jnp.int32)
    kept = jnp.clip((counts[:, None] - groups[None, :] + dp - 1) // dp, 0, per)
    ends = jnp.cumsum(kept, axis=0)
    starts = ends - kept

    my_ends = ends[:, group]
    my_starts = starts[:, group]
    rows = jnp.arange(cap, dtype=jnp.int32)
    slot_of = jnp.sum((my_ends[None, :] <= rows[:, None]).astype(jnp.int32), axis=1)
    in_use = slot_of < nseq
    slot_c = jnp.minimum(slot_of, nseq - 1)
    src = jnp.clip(slot_c * per + rows - my_starts[slot_c], 0, nseq * per - 1)

    grads_r = redistribute(out_grads, dp)
    grads_p = jnp.take(grads_r, src, axis=0, mode="clip")
    grads_p = jnp.where(in_use[:, None], grads_p, jnp.zeros_like(grads_p))
    acts_r = redistribute(acts, dp)
    acts_p = jnp.take(acts_r, src, axis=0, mode="clip")

    act_part = jnp.dot(acts_p, basis_in, preferred_element_type=jnp.float32)
    act_sum = lax.psum_scatter(act_part, "tensor", scatter_dimension=1, tiled=True).astype(jnp.bfloat16)
    grad_part = jnp.dot(grads_p, basis_out, preferred_element_type=jnp.float32)
    grad_part, act_sum = lax.optimization_barrier((grad_part, act_sum))
    quarter = act_sum.shape[1]
    sent = jnp.broadcast_to(act_sum[None], (tp,) + act_sum.shape).reshape(-1, quarter)
    act_whole = lax.all_to_all(sent, "tensor", 0, 0, tiled=True).reshape(tp, cap, quarter)
    act_whole = act_whole.transpose(1, 0, 2).reshape(cap, tp * quarter)
    in_cols = act_whole.shape[1] // dp
    act_whole = act_whole.reshape(cap, dp, in_cols).transpose(1, 0, 2).reshape(-1, in_cols)
    rot_acts = lax.all_to_all(act_whole, "dp", 0, 0, tiled=True)

    rot_grads = lax.psum_scatter(grad_part, "tensor", scatter_dimension=1, tiled=True)
    rot_grads, rot_acts = lax.optimization_barrier((rot_grads, rot_acts))
    rot_grads = rot_grads.astype(jnp.bfloat16)
    all_grads = lax.all_gather(rot_grads, "dp", axis=0, tiled=True)

    span = per + 16
    lo = groups[None, :] * cap + starts
    win = jnp.minimum((lo // 16) * 16, dp * cap - span)
    out_rows, in_cols = all_grads.shape[1], rot_acts.shape[1]
    pair = 2 if nseq % 2 == 0 else 1
    kernel = functools.partial(slot_squares, dp=dp, per=span, pair=pair, scale=1.0 / (nseq * LEN))
    return pl.pallas_call(
        kernel,
        out_shape=jax.ShapeDtypeStruct((out_rows, in_cols), jnp.float32),
        grid_spec=pltpu.PrefetchScalarGridSpec(
            num_scalar_prefetch=3,
            grid=(nseq // pair,),
            in_specs=[pl.BlockSpec(memory_space=pl.ANY), pl.BlockSpec(memory_space=pl.ANY)],
            out_specs=pl.BlockSpec((out_rows, in_cols), lambda s, *_: (0, 0)),
            scratch_shapes=[
                pltpu.VMEM((2, pair, dp * span, out_rows), jnp.bfloat16),
                pltpu.VMEM((2, pair, dp * span, in_cols), jnp.bfloat16),
                pltpu.SemaphoreType.DMA((2, pair, 2, dp)),
            ],
        ),
        compiler_params=pltpu.CompilerParams(dimension_semantics=("arbitrary",)),
    )(win.reshape(-1), lo.reshape(-1), (lo + kept).reshape(-1), all_grads, rot_acts)


def solution(mesh):
    dp = mesh.shape["dp"]
    tp = mesh.shape["tensor"]

    def body(*args):
        return shards(*args, dp=dp, tp=tp)

    return jax.shard_map(
        body,
        mesh=mesh,
        in_specs=(
            P("dp", "tensor"),
            P("dp", "tensor"),
            P("tensor", None),
            P("tensor", None),
            P(),
            P(),
        ),
        out_specs=P("tensor", "dp"),
        check_vma=False,
    )
```

```python
import functools

import jax
import jax.numpy as jnp
from jax import lax
from jax.experimental import pallas as pl
from jax.experimental.pallas import tpu as pltpu
from jax.sharding import PartitionSpec as P

LEN = 256
VALID_NUM, VALID_DEN = 5, 8


def redistribute(x, dp):
    slots = x.shape[0] // LEN
    width = x.shape[1]
    x = x.reshape(slots, LEN // dp, dp, width).transpose(2, 0, 1, 3).reshape(-1, width)
    return lax.all_to_all(x, "dp", 0, 0, tiled=True)


def slot_squares(win_ref, lo_ref, hi_ref, grads_hbm, acts_hbm, out_ref, gbuf, abuf, sems, *, dp, per, pair, scale):
    s = pl.program_id(0)
    n = pl.num_programs(0)

    def copies(step, b):
        out = []
        for q in range(pair):
            for g in range(dp):
                w = pl.multiple_of(win_ref[(step * pair + q) * dp + g], 16)
                rows = pl.ds(g * per, per)
                out.append(pltpu.make_async_copy(grads_hbm.at[pl.ds(w, per)], gbuf.at[b, q, rows], sems.at[b, q, 0, g]))
                out.append(pltpu.make_async_copy(acts_hbm.at[pl.ds(w, per)], abuf.at[b, q, rows], sems.at[b, q, 1, g]))
        return out

    b = s % 2

    @pl.when(s == 0)
    def _():
        for c in copies(0, 0):
            c.start()

    @pl.when(s + 1 < n)
    def _():
        for c in copies(s + 1, 1 - b):
            c.start()

    for c in copies(s, b):
        c.wait()

    @pl.when(s == 0)
    def _():
        out_ref[...] = jnp.zeros_like(out_ref)

    acc = None
    for q in range(pair):
        slot = s * pair + q
        for g in range(dp):
            row = win_ref[slot * dp + g] + lax.broadcasted_iota(jnp.int32, (per, 1), 0)
            keep = (row >= lo_ref[slot * dp + g]) & (row < hi_ref[slot * dp + g])
            a = abuf[b, q, pl.ds(g * per, per), :].astype(jnp.float32)
            abuf[b, q, pl.ds(g * per, per), :] = jnp.where(keep, a, 0.0).astype(jnp.bfloat16)
        rotated = lax.dot_general(
            gbuf[b, q], abuf[b, q], (((0,), (0,)), ((), ())), preferred_element_type=jnp.float32
        )
        acc = rotated * rotated if acc is None else acc + rotated * rotated
    out_ref[...] += acc

    @pl.when(s == n - 1)
    def _():
        out_ref[...] = out_ref[...] * scale


def shards(acts, out_grads, basis_out, basis_in, slot_sequence, seq_lengths, *, dp, tp):
    tok_rows = acts.shape[0]
    local_slots = tok_rows // LEN
    nseq = seq_lengths.shape[0]
    per = LEN // dp
    total = nseq * LEN * VALID_NUM // VALID_DEN
    cap = -(-(total + nseq * (dp - 1)) // dp)
    cap = -(-cap // 16) * 16
    group = lax.axis_index("dp")

    counts = seq_lengths[slot_sequence]
    groups = jnp.arange(dp, dtype=jnp.int32)
    kept = jnp.clip((counts[:, None] - groups[None, :] + dp - 1) // dp, 0, per)
    ends = jnp.cumsum(kept, axis=0)
    starts = ends - kept

    my_ends = ends[:, group]
    my_starts = starts[:, group]
    rows = jnp.arange(cap, dtype=jnp.int32)
    slot_of = jnp.sum((my_ends[None, :] <= rows[:, None]).astype(jnp.int32), axis=1)
    in_use = slot_of < nseq
    slot_c = jnp.minimum(slot_of, nseq - 1)
    src = jnp.clip(slot_c * per + rows - my_starts[slot_c], 0, nseq * per - 1)

    grads_r = redistribute(out_grads, dp)
    grads_p = jnp.take(grads_r, src, axis=0, mode="clip")
    grads_p = jnp.where(in_use[:, None], grads_p, jnp.zeros_like(grads_p))
    acts_r = redistribute(acts, dp)
    acts_p = jnp.take(acts_r, src, axis=0, mode="clip")

    quarter = basis_in.shape[1] // tp
    basis_cols = basis_in.reshape(basis_in.shape[0], tp, quarter).transpose(1, 0, 2).reshape(-1, quarter)
    basis_q = lax.all_to_all(basis_cols, "tensor", 0, 0, tiled=True)
    copies = jnp.broadcast_to(acts_p[None], (tp,) + acts_p.shape).reshape(-1, acts_p.shape[1])
    acts_full = lax.all_to_all(copies, "tensor", 0, 0, tiled=True).reshape(tp, cap, acts_p.shape[1])
    acts_full = acts_full.transpose(1, 0, 2).reshape(cap, -1)
    act_sum = jnp.dot(acts_full, basis_q, preferred_element_type=jnp.float32).astype(jnp.bfloat16)
    grad_part = jnp.dot(grads_p, basis_out, preferred_element_type=jnp.float32)
    grad_part, act_sum = lax.optimization_barrier((grad_part, act_sum))
    quarter = act_sum.shape[1]
    sent = jnp.broadcast_to(act_sum[None], (tp,) + act_sum.shape).reshape(-1, quarter)
    act_whole = lax.all_to_all(sent, "tensor", 0, 0, tiled=True).reshape(tp, cap, quarter)
    act_whole = act_whole.transpose(1, 0, 2).reshape(cap, tp * quarter)
    in_cols = act_whole.shape[1] // dp
    act_whole = act_whole.reshape(cap, dp, in_cols).transpose(1, 0, 2).reshape(-1, in_cols)
    rot_acts = lax.all_to_all(act_whole, "dp", 0, 0, tiled=True)

    rot_grads = lax.psum_scatter(grad_part, "tensor", scatter_dimension=1, tiled=True)
    rot_grads, rot_acts = lax.optimization_barrier((rot_grads, rot_acts))
    rot_grads = rot_grads.astype(jnp.bfloat16)
    all_grads = lax.all_gather(rot_grads, "dp", axis=0, tiled=True)

    span = per + 16
    lo = groups[None, :] * cap + starts
    win = jnp.minimum((lo // 16) * 16, dp * cap - span)
    out_rows, in_cols = all_grads.shape[1], rot_acts.shape[1]
    pair = 2 if nseq % 2 == 0 else 1
    kernel = functools.partial(slot_squares, dp=dp, per=span, pair=pair, scale=1.0 / (nseq * LEN))
    return pl.pallas_call(
        kernel,
        out_shape=jax.ShapeDtypeStruct((out_rows, in_cols), jnp.float32),
        grid_spec=pltpu.PrefetchScalarGridSpec(
            num_scalar_prefetch=3,
            grid=(nseq // pair,),
            in_specs=[pl.BlockSpec(memory_space=pl.ANY), pl.BlockSpec(memory_space=pl.ANY)],
            out_specs=pl.BlockSpec((out_rows, in_cols), lambda s, *_: (0, 0)),
            scratch_shapes=[
                pltpu.VMEM((2, pair, dp * span, out_rows), jnp.bfloat16),
                pltpu.VMEM((2, pair, dp * span, in_cols), jnp.bfloat16),
                pltpu.SemaphoreType.DMA((2, pair, 2, dp)),
            ],
        ),
        compiler_params=pltpu.CompilerParams(dimension_semantics=("arbitrary",)),
    )(win.reshape(-1), lo.reshape(-1), (lo + kept).reshape(-1), all_grads, rot_acts)


def solution(mesh):
    dp = mesh.shape["dp"]
    tp = mesh.shape["tensor"]

    def body(*args):
        return shards(*args, dp=dp, tp=tp)

    return jax.shard_map(
        body,
        mesh=mesh,
        in_specs=(
            P("dp", "tensor"),
            P("dp", "tensor"),
            P("tensor", None),
            P("tensor", None),
            P(),
            P(),
        ),
        out_specs=P("tensor", "dp"),
        check_vma=False,
    )
```

```python
import functools

import jax
import jax.numpy as jnp
from jax import lax
from jax.experimental import pallas as pl
from jax.experimental.pallas import tpu as pltpu
from jax.sharding import PartitionSpec as P

LEN = 256
VALID_NUM, VALID_DEN = 5, 8


def redistribute(x, dp):
    slots = x.shape[0] // LEN
    width = x.shape[1]
    x = x.reshape(slots, LEN // dp, dp, width).transpose(2, 0, 1, 3).reshape(-1, width)
    return lax.all_to_all(x, "dp", 0, 0, tiled=True)


def slot_squares(win_ref, lo_ref, hi_ref, grads_hbm, acts_hbm, out_ref, gbuf, abuf, sems, *, dp, per, pair, scale):
    s = pl.program_id(0)
    n = pl.num_programs(0)

    def copies(step, b):
        out = []
        for q in range(pair):
            for g in range(dp):
                w = pl.multiple_of(win_ref[(step * pair + q) * dp + g], 16)
                rows = pl.ds(g * per, per)
                out.append(pltpu.make_async_copy(grads_hbm.at[pl.ds(w, per)], gbuf.at[b, q, rows], sems.at[b, q, 0, g]))
                out.append(pltpu.make_async_copy(acts_hbm.at[pl.ds(w, per)], abuf.at[b, q, rows], sems.at[b, q, 1, g]))
        return out

    b = s % 2

    @pl.when(s == 0)
    def _():
        for c in copies(0, 0):
            c.start()

    @pl.when(s + 1 < n)
    def _():
        for c in copies(s + 1, 1 - b):
            c.start()

    for c in copies(s, b):
        c.wait()

    @pl.when(s == 0)
    def _():
        out_ref[...] = jnp.zeros_like(out_ref)

    acc = None
    for q in range(pair):
        slot = s * pair + q
        for g in range(dp):
            row = win_ref[slot * dp + g] + lax.broadcasted_iota(jnp.int32, (per, 1), 0)
            keep = (row >= lo_ref[slot * dp + g]) & (row < hi_ref[slot * dp + g])
            a = abuf[b, q, pl.ds(g * per, per), :].astype(jnp.float32)
            abuf[b, q, pl.ds(g * per, per), :] = jnp.where(keep, a, 0.0).astype(jnp.bfloat16)
        rotated = lax.dot_general(
            gbuf[b, q], abuf[b, q], (((0,), (0,)), ((), ())), preferred_element_type=jnp.float32
        )
        acc = rotated * rotated if acc is None else acc + rotated * rotated
    out_ref[...] += acc

    @pl.when(s == n - 1)
    def _():
        out_ref[...] = out_ref[...] * scale


def shards(acts, out_grads, basis_out, basis_in, slot_sequence, seq_lengths, *, dp, tp):
    tok_rows = acts.shape[0]
    local_slots = tok_rows // LEN
    nseq = seq_lengths.shape[0]
    per = LEN // dp
    total = nseq * LEN * VALID_NUM // VALID_DEN
    cap = -(-(total + nseq * (dp - 1)) // dp)
    cap = -(-cap // 16) * 16
    group = lax.axis_index("dp")

    counts = seq_lengths[slot_sequence]
    groups = jnp.arange(dp, dtype=jnp.int32)
    kept = jnp.clip((counts[:, None] - groups[None, :] + dp - 1) // dp, 0, per)
    ends = jnp.cumsum(kept, axis=0)
    starts = ends - kept

    my_ends = ends[:, group]
    my_starts = starts[:, group]
    rows = jnp.arange(cap, dtype=jnp.int32)
    slot_of = jnp.sum((my_ends[None, :] <= rows[:, None]).astype(jnp.int32), axis=1)
    in_use = slot_of < nseq
    slot_c = jnp.minimum(slot_of, nseq - 1)
    src = jnp.clip(slot_c * per + rows - my_starts[slot_c], 0, nseq * per - 1)

    grads_r = redistribute(out_grads, dp)
    grads_p = jnp.take(grads_r, src, axis=0, mode="clip")
    grads_p = jnp.where(in_use[:, None], grads_p, jnp.zeros_like(grads_p))
    acts_r = redistribute(acts, dp)
    acts_p = jnp.take(acts_r, src, axis=0, mode="clip")

    act_part = jnp.dot(acts_p, basis_in, preferred_element_type=jnp.float32)
    act_sum = lax.psum_scatter(act_part, "tensor", scatter_dimension=1, tiled=True).astype(jnp.bfloat16)
    grad_part = jnp.dot(grads_p, basis_out, preferred_element_type=jnp.float32)
    grad_part, act_sum = lax.optimization_barrier((grad_part, act_sum))
    quarter = act_sum.shape[1]
    sent = jnp.broadcast_to(act_sum[None], (tp,) + act_sum.shape).reshape(-1, quarter)
    act_whole = lax.all_to_all(sent, "tensor", 0, 0, tiled=True).reshape(tp, cap, quarter)
    act_whole = act_whole.transpose(1, 0, 2).reshape(cap, tp * quarter)
    in_cols = act_whole.shape[1] // dp
    act_whole = act_whole.reshape(cap, dp, in_cols).transpose(1, 0, 2).reshape(-1, in_cols)
    rot_acts = lax.all_to_all(act_whole, "dp", 0, 0, tiled=True)

    rot_grads = lax.psum_scatter(grad_part, "tensor", scatter_dimension=1, tiled=True)
    rot_grads, rot_acts = lax.optimization_barrier((rot_grads, rot_acts))
    rot_grads = rot_grads.astype(jnp.bfloat16)
    all_grads = lax.all_gather(rot_grads, "dp", axis=0, tiled=True)

    span = per + 16
    lo = groups[None, :] * cap + starts
    win = jnp.minimum((lo // 16) * 16, dp * cap - span)
    out_rows, in_cols = all_grads.shape[1], rot_acts.shape[1]
    pair = 4 if nseq % 4 == 0 else 1
    kernel = functools.partial(slot_squares, dp=dp, per=span, pair=pair, scale=1.0 / (nseq * LEN))
    return pl.pallas_call(
        kernel,
        out_shape=jax.ShapeDtypeStruct((out_rows, in_cols), jnp.float32),
        grid_spec=pltpu.PrefetchScalarGridSpec(
            num_scalar_prefetch=3,
            grid=(nseq // pair,),
            in_specs=[pl.BlockSpec(memory_space=pl.ANY), pl.BlockSpec(memory_space=pl.ANY)],
            out_specs=pl.BlockSpec((out_rows, in_cols), lambda s, *_: (0, 0)),
            scratch_shapes=[
                pltpu.VMEM((2, pair, dp * span, out_rows), jnp.bfloat16),
                pltpu.VMEM((2, pair, dp * span, in_cols), jnp.bfloat16),
                pltpu.SemaphoreType.DMA((2, pair, 2, dp)),
            ],
        ),
        compiler_params=pltpu.CompilerParams(dimension_semantics=("arbitrary",)),
    )(win.reshape(-1), lo.reshape(-1), (lo + kept).reshape(-1), all_grads, rot_acts)


def solution(mesh):
    dp = mesh.shape["dp"]
    tp = mesh.shape["tensor"]

    def body(*args):
        return shards(*args, dp=dp, tp=tp)

    return jax.shard_map(
        body,
        mesh=mesh,
        in_specs=(
            P("dp", "tensor"),
            P("dp", "tensor"),
            P("tensor", None),
            P("tensor", None),
            P(),
            P(),
        ),
        out_specs=P("tensor", "dp"),
        check_vma=False,
    )
```

```python
import functools

import jax
import jax.numpy as jnp
from jax import lax
from jax.experimental import pallas as pl
from jax.experimental.pallas import tpu as pltpu
from jax.sharding import PartitionSpec as P

LEN = 256
VALID_NUM, VALID_DEN = 5, 8


def redistribute(x, dp):
    slots = x.shape[0] // LEN
    width = x.shape[1]
    x = x.reshape(slots, LEN // dp, dp, width).transpose(2, 0, 1, 3).reshape(-1, width)
    return lax.all_to_all(x, "dp", 0, 0, tiled=True)


def slot_squares(win_ref, lo_ref, hi_ref, grads_hbm, acts_hbm, out_ref, gbuf, abuf, sems, *, dp, per, pair, scale):
    s = pl.program_id(0)
    n = pl.num_programs(0)

    def copies(step, b):
        out = []
        for q in range(pair):
            for g in range(dp):
                w = pl.multiple_of(win_ref[(step * pair + q) * dp + g], 16)
                rows = pl.ds(g * per, per)
                out.append(pltpu.make_async_copy(grads_hbm.at[pl.ds(w, per)], gbuf.at[b, q, rows], sems.at[b, q, 0, g]))
                out.append(pltpu.make_async_copy(acts_hbm.at[pl.ds(w, per)], abuf.at[b, q, rows], sems.at[b, q, 1, g]))
        return out

    b = s % 2

    @pl.when(s == 0)
    def _():
        for c in copies(0, 0):
            c.start()

    @pl.when(s + 1 < n)
    def _():
        for c in copies(s + 1, 1 - b):
            c.start()

    for c in copies(s, b):
        c.wait()

    @pl.when(s == 0)
    def _():
        out_ref[...] = jnp.zeros_like(out_ref)

    acc = None
    for q in range(pair):
        slot = s * pair + q
        for g in range(dp):
            row = win_ref[slot * dp + g] + lax.broadcasted_iota(jnp.int32, (per, 1), 0)
            keep = (row >= lo_ref[slot * dp + g]) & (row < hi_ref[slot * dp + g])
            a = abuf[b, q, pl.ds(g * per, per), :].astype(jnp.float32)
            abuf[b, q, pl.ds(g * per, per), :] = jnp.where(keep, a, 0.0).astype(jnp.bfloat16)
        rotated = lax.dot_general(
            gbuf[b, q], abuf[b, q], (((0,), (0,)), ((), ())), preferred_element_type=jnp.float32
        )
        acc = rotated * rotated if acc is None else acc + rotated * rotated
    out_ref[...] += acc

    @pl.when(s == n - 1)
    def _():
        out_ref[...] = out_ref[...] * scale


def shards(acts, out_grads, basis_out, basis_in, slot_sequence, seq_lengths, *, dp, tp):
    tok_rows = acts.shape[0]
    local_slots = tok_rows // LEN
    nseq = seq_lengths.shape[0]
    per = LEN // dp
    total = nseq * LEN * VALID_NUM // VALID_DEN
    cap = -(-(total + nseq * (dp - 1)) // dp)
    cap = -(-cap // 16) * 16
    group = lax.axis_index("dp")

    counts = seq_lengths[slot_sequence]
    groups = jnp.arange(dp, dtype=jnp.int32)
    kept = jnp.clip((counts[:, None] - groups[None, :] + dp - 1) // dp, 0, per)
    ends = jnp.cumsum(kept, axis=0)
    starts = ends - kept

    my_ends = ends[:, group]
    my_starts = starts[:, group]
    rows = jnp.arange(cap, dtype=jnp.int32)
    slot_of = jnp.sum((my_ends[None, :] <= rows[:, None]).astype(jnp.int32), axis=1)
    in_use = slot_of < nseq
    slot_c = jnp.minimum(slot_of, nseq - 1)
    src = jnp.clip(slot_c * per + rows - my_starts[slot_c], 0, nseq * per - 1)

    grads_r = redistribute(out_grads, dp)
    grads_p = jnp.take(grads_r, src, axis=0, mode="clip")
    grads_p = jnp.where(in_use[:, None], grads_p, jnp.zeros_like(grads_p))
    acts_r = redistribute(acts, dp)
    acts_p = jnp.take(acts_r, src, axis=0, mode="clip")

    act_part = jnp.dot(acts_p, basis_in, preferred_element_type=jnp.float32)
    act_sum = lax.psum_scatter(act_part, "tensor", scatter_dimension=1, tiled=True).astype(jnp.bfloat16)
    grad_part = jnp.dot(grads_p, basis_out, preferred_element_type=jnp.float32)
    grad_part, act_sum = lax.optimization_barrier((grad_part, act_sum))
    quarter = act_sum.shape[1]
    sent = jnp.broadcast_to(act_sum[None], (tp,) + act_sum.shape).reshape(-1, quarter)
    act_whole = lax.all_to_all(sent, "tensor", 0, 0, tiled=True).reshape(tp, cap, quarter)
    act_whole = act_whole.transpose(1, 0, 2).reshape(cap, tp * quarter)
    in_cols = act_whole.shape[1] // dp
    act_whole = act_whole.reshape(cap, dp, in_cols).transpose(1, 0, 2).reshape(-1, in_cols)
    rot_acts = lax.all_to_all(act_whole, "dp", 0, 0, tiled=True)

    rot_grads = lax.psum_scatter(grad_part, "tensor", scatter_dimension=1, tiled=True)
    rot_grads, rot_acts = lax.optimization_barrier((rot_grads, rot_acts))
    rot_grads = rot_grads.astype(jnp.bfloat16)
    all_grads = lax.all_gather(rot_grads, "dp", axis=0, tiled=True)

    span = per + 16
    lo = groups[None, :] * cap + starts
    win = jnp.minimum((lo // 16) * 16, dp * cap - span)
    out_rows, in_cols = all_grads.shape[1], rot_acts.shape[1]
    pair = 8 if nseq % 8 == 0 else 1
    kernel = functools.partial(slot_squares, dp=dp, per=span, pair=pair, scale=1.0 / (nseq * LEN))
    return pl.pallas_call(
        kernel,
        out_shape=jax.ShapeDtypeStruct((out_rows, in_cols), jnp.float32),
        grid_spec=pltpu.PrefetchScalarGridSpec(
            num_scalar_prefetch=3,
            grid=(nseq // pair,),
            in_specs=[pl.BlockSpec(memory_space=pl.ANY), pl.BlockSpec(memory_space=pl.ANY)],
            out_specs=pl.BlockSpec((out_rows, in_cols), lambda s, *_: (0, 0)),
            scratch_shapes=[
                pltpu.VMEM((2, pair, dp * span, out_rows), jnp.bfloat16),
                pltpu.VMEM((2, pair, dp * span, in_cols), jnp.bfloat16),
                pltpu.SemaphoreType.DMA((2, pair, 2, dp)),
            ],
        ),
        compiler_params=pltpu.CompilerParams(dimension_semantics=("arbitrary",)),
    )(win.reshape(-1), lo.reshape(-1), (lo + kept).reshape(-1), all_grads, rot_acts)


def solution(mesh):
    dp = mesh.shape["dp"]
    tp = mesh.shape["tensor"]

    def body(*args):
        return shards(*args, dp=dp, tp=tp)

    return jax.shard_map(
        body,
        mesh=mesh,
        in_specs=(
            P("dp", "tensor"),
            P("dp", "tensor"),
            P("tensor", None),
            P("tensor", None),
            P(),
            P(),
        ),
        out_specs=P("tensor", "dp"),
        check_vma=False,
    )
```
